256 devices in a mesh: dp: 4 (over x), expert: 64 (over y, z, core).
Axes of the slice: x: 4, y: 4, z: 8, core: 2. Of those that a mesh axis runs over, the one named last changes fastest.
Arguments:
- tokens: bfloat16 [32768, 2048], P(('dp', 'expert')), may hold values from -6 to 6
- expert_ids: int32 [32768, 8], P(('dp', 'expert')), may hold values from 0 to 63, all different within a row; in each aligned block of 128 rows (0 to 127, 128 to 255, ...) at most 24 rows name the same one
- gate_probs: float32 [32768, 8], P(('dp', 'expert')), may hold values from 0.02 to 1
- placement: int32 [64], replicated, may hold values from 0 to 63, each once
- w_gate_up: bfloat16 [64, 2, 768, 2048], P('expert', None, 'dp'), may hold values from -0.125 to 0.125
- w_down: bfloat16 [64, 768, 2048], P('expert', 'dp'), may hold values from -0.21875 to 0.21875
Outputs:
- critic_mix: bfloat16 [32768, 2048], P(('dp', 'expert'))
- placed_gate_up: bfloat16 [64, 2, 768, 2048], P('expert', None, 'dp')
- placed_down: bfloat16 [64, 768, 2048], P('expert', 'dp')
The draws below stay inside these ranges and needn't reach their ends.
Inputs may be any that keep to these rules, and one draw needn't show every extreme that they name: `expert_ids`: each token names 8 different experts; among the 128 tokens of one device at most 24 name the same expert, and some device reaches 24. `placement`: A permutation of the expert numbers.
All inputs are finite; a program needn't handle non-finite values.
Results may differ from the reference program's by a relative error of at most 0.0058.
Values may be sent and summed in bfloat16 or wider, within the bound.
No kernel may reach another device: no remote copies, remote signals or barrier semaphores. Data moves between devices by JAX's collectives and lax.ppermute only.
A program may use at most 128 MiB of HBM per device.

```python
import math
import jax
import jax.numpy as jnp
import numpy as np
from jax import lax

D = 2048
FF = 768
TOP = 8
TOK_DEV = 128
EXPERTS = 64
CAP = 24
TOKENS = 32768


def block_levels(own_key, extent, split, low, largest):
    factor_of, own = 1.0, jax.random.fold_in(own_key, 6)
    for dim, parts in split:
        steps = jnp.exp(jax.random.uniform(jax.random.fold_in(own, dim), (parts,), jnp.float32, low / len(split), largest / len(split)))
        factor_of = factor_of * jnp.repeat(steps, extent[dim] // parts).reshape([-1 if axis == dim else 1 for axis in range(len(extent))])
    return factor_of


def shared_out(key, own, number, rows, amount, top, most, lean):
    order = jax.random.permutation(key, amount)
    heavy_load, ordinary = portions_of(amount, rows * top, most, lean, True), portions_of(amount, rows * top, most, lean, False)
    places = jnp.arange(amount)

    def named(lengths, rotation):
        used = int((lengths > 0).sum())
        fixed = max(1, used // 4)
        shifted = fixed + (places - fixed + rotation * (used - fixed)) % max(1, amount - fixed)
        return jnp.zeros((amount,), jnp.int32).at[order[jnp.where(places < fixed, places, shifted)]].set(jnp.asarray(lengths, jnp.int32))

    lengths = jnp.where(number % 4 == 0, named(heavy_load, number // 4), named(ordinary, number - number // 4 - 1))
    mixed = jax.random.permutation(jax.random.fold_in(own, 3), amount)
    source_of, taker = mixed[0:amount // 2 * 2:2], mixed[1:amount // 2 * 2:2]
    room = jnp.minimum(lengths[source_of] - 1, most - lengths[taker]) // 2
    room = jnp.where((source_of == order[0]) | (taker == order[0]) | (lengths[taker] == 0), 0, jnp.maximum(room, 0))
    shifted = jax.random.randint(jax.random.fold_in(own, 4), (amount // 2,), 0, 1 << 20) % (room + 1)
    lengths = lengths.at[source_of].add(-shifted).at[taker].add(shifted)
    members = jnp.searchsorted(jnp.cumsum(lengths), jnp.arange(rows * top), side="right").astype(jnp.int32)
    grid = members.reshape(top, rows).T
    grid = grid[jax.random.permutation(jax.random.fold_in(own, 1), rows)]
    rotation = jax.random.randint(jax.random.fold_in(own, 2), (rows, 1), 0, top)
    return jnp.take_along_axis(grid, (jnp.arange(top)[None, :] + rotation) % top, axis=1)


def portions_of(number_of, total, bound, skew, full):
    weights = [(1 << 20) // math.isqrt(grade ** skew) + 1 for grade in range(1, number_of + 1)]
    largest = bound if full else min(bound, max(-(-total // number_of), total * weights[0] // sum(weights)))
    least = 1 if total - largest >= number_of - 1 else 0
    counts, rest = [largest] + [least] * (number_of - 1), total - largest - least * (number_of - 1)
    while rest > 0:
        movable = [i for i in range(1, number_of) if counts[i] < largest] or [i for i in range(1, number_of) if counts[i] < bound]
        mass, budget = sum([weights[i] for i in movable]), rest
        for i in movable:
            extra = min(bound - counts[i], max(1, budget * weights[i] // mass), rest)
            counts[i] = counts[i] + extra
            rest = rest - extra
    return np.array(counts)


def scatter_about(stream_key, extent, deviation, most, pieces=(), kind=jnp.bfloat16):
    gain = block_levels(stream_key, extent, pieces, -0.22, 0.18) if pieces else 1.0
    drawn = jax.random.normal(stream_key, extent, jnp.float32) * deviation * gain
    return jnp.minimum(jnp.maximum(drawn, -most), most).astype(kind)


def setup_inputs(seed: int = 0) -> dict:
    keys = jax.random.split(jax.random.key(seed), 7)
    tokens = scatter_about(keys[0], (TOKENS, D), 1.0, 6.0, ((0, 256),))
    expert_ids_keys = jax.random.split(jax.random.fold_in(keys[1], 1), TOKENS // TOK_DEV)
    expert_ids_turns = jax.random.permutation(jax.random.fold_in(keys[1], 3), TOKENS // TOK_DEV)
    expert_ids = jax.vmap(lambda own, number: shared_out(jax.random.fold_in(keys[1], 2), own, number, TOK_DEV, EXPERTS, TOP, CAP, 2))(expert_ids_keys, expert_ids_turns).reshape((TOKENS, TOP))
    gate_probs = jnp.clip(jnp.exp(math.log(1.0) - 3.912023 * jax.random.uniform(keys[2], (TOKENS, TOP), jnp.float32) ** block_levels(keys[2], (TOKENS, TOP), ((0, 256),), -0.2, 0.2)), 0.02, 1.0)
    placement = jax.random.permutation(keys[3], EXPERTS).astype(jnp.int32)
    w_gate_up = scatter_about(keys[4], (EXPERTS, 2, FF, D), D ** -0.5, 0.125, ((0, 64), (2, 4)))
    w_down = scatter_about(keys[5], (EXPERTS, FF, D), FF ** -0.5, 0.21875, ((0, 64), (1, 4)))
    return {"tokens": tokens, "expert_ids": expert_ids, "gate_probs": gate_probs, "placement": placement, "w_gate_up": w_gate_up, "w_down": w_down}


def reference(tokens, expert_ids, gate_probs, placement, w_gate_up, w_down):
    token_total = tokens.shape[0]
    experts = placement.shape[0]
    blocks = token_total // TOK_DEV
    numbers = jnp.arange(experts, dtype=jnp.int32)
    inverse = jnp.zeros((experts,), jnp.int32).at[placement].set(numbers)
    placed_gate_up = w_gate_up[inverse]
    placed_down = w_down[inverse]
    gates = gate_probs / jnp.sum(gate_probs, axis=1, keepdims=True)
    block_ids = expert_ids.reshape(blocks, TOK_DEV * TOP)
    onehot = (block_ids[:, :, None] == numbers[None, None, :]).astype(jnp.int32)
    before = jnp.cumsum(onehot, axis=1) - onehot
    slot_of = jnp.sum(before * onehot, axis=2).reshape(-1)
    flat_ids = expert_ids.reshape(-1)
    flat_gates = gates.reshape(-1)
    assign = jnp.arange(token_total * TOP, dtype=jnp.int32)
    position = (assign // (TOK_DEV * TOP)) * CAP + slot_of
    token_of = assign // TOP
    padded = jnp.concatenate([tokens, jnp.zeros((1, D), tokens.dtype)], axis=0)
    slot_total = blocks * CAP

    def one_expert(summed, expert_pos):
        chosen = flat_ids == expert_pos
        where_to = jnp.where(chosen, position, slot_total)
        rows_of = jnp.full((slot_total,), token_total, jnp.int32).at[where_to].set(token_of, mode="drop")
        gate_of = jnp.zeros((slot_total,), jnp.float32).at[where_to].set(flat_gates, mode="drop")
        row_block = padded[rows_of].astype(jnp.float32)
        source = inverse[expert_pos]
        pair = w_gate_up[source].astype(jnp.float32)
        gate_part = jnp.dot(row_block, pair[0].T, preferred_element_type=jnp.float32)
        up_part = jnp.dot(row_block, pair[1].T, preferred_element_type=jnp.float32)
        hidden = (jax.nn.silu(gate_part) * up_part).astype(jnp.bfloat16)
        result = jnp.dot(hidden.astype(jnp.float32), w_down[source].astype(jnp.float32), preferred_element_type=jnp.float32).astype(jnp.bfloat16)
        summed = summed.at[rows_of].add(gate_of[:, None] * result.astype(jnp.float32), mode="drop")
        return summed, None

    summed, _ = lax.scan(one_expert, jnp.zeros((token_total, D), jnp.float32), numbers)
    return summed.astype(jnp.bfloat16), placed_gate_up, placed_down
```

```python
import jax
import jax.numpy as jnp
from jax import lax
from jax.sharding import PartitionSpec as P


def per_device(tokens, expert_ids, gate_probs, placement, w_gate_up, w_down):
    tok_dev = tokens.shape[0]
    model_width = tokens.shape[1]
    top_count = expert_ids.shape[1]
    experts = placement.shape[0]
    capacity = min(tok_dev, 3 * tok_dev * top_count // (2 * experts))
    numbers = jnp.arange(experts, dtype=jnp.int32)
    inverse = jnp.sum(
        jnp.where(placement[:, None] == numbers[None, :], numbers[:, None], 0), axis=0
    )
    flat_ids = jnp.take(inverse, expert_ids.reshape(-1), axis=0)
    onehot = (flat_ids[:, None] == numbers[None, :]).astype(jnp.int32)
    before = jnp.cumsum(onehot, axis=0) - onehot
    slot_of = jnp.sum(before * onehot, axis=1)
    down_four = w_down.reshape((1, 1) + w_down.shape[1:])
    pieces = (
        lax.all_to_all(w_gate_up, "expert", split_axis=3, concat_axis=0, tiled=True),
        lax.all_to_all(down_four, "expert", split_axis=3, concat_axis=0, tiled=True),
    )
    reordered = (jnp.take(pieces[0], inverse, axis=0), jnp.take(pieces[1], inverse, axis=0))
    placed = (
        lax.all_to_all(reordered[0], "expert", split_axis=0, concat_axis=3, tiled=True),
        lax.all_to_all(reordered[1], "expert", split_axis=0, concat_axis=3, tiled=True),
    )
    placed_gate_up = placed[0]
    placed_down = placed[1].reshape(w_down.shape)
    gathered = (
        lax.all_gather(w_gate_up, "dp", axis=2, tiled=True),
        lax.all_gather(w_down, "dp", axis=1, tiled=True),
    )
    hidden_count = gathered[0].shape[2]
    gate_up_full = gathered[0].reshape(2 * hidden_count, model_width)
    down_full = gathered[1].reshape(hidden_count, model_width)
    flat_index = flat_ids * capacity + slot_of
    spread_rows = jnp.broadcast_to(tokens[:, None, :], (tok_dev, top_count, model_width)).reshape(
        -1, model_width
    )
    buffer = (
        jnp.zeros((experts * capacity, model_width), jnp.bfloat16).at[flat_index].set(spread_rows)
    )
    buffer = buffer.reshape(experts, capacity, model_width)
    received = lax.all_to_all(buffer, "expert", split_axis=0, concat_axis=0, tiled=True)
    row_block = received.reshape(-1, model_width)
    projected = lax.dot_general(
        row_block, gate_up_full, (((1,), (1,)), ((), ())), preferred_element_type=jnp.float32
    )
    gate_part = projected[:, :hidden_count]
    up_part = projected[:, hidden_count:]
    hidden = (jax.nn.silu(gate_part) * up_part).astype(jnp.bfloat16)
    result = jnp.dot(hidden, down_full, preferred_element_type=jnp.float32).astype(jnp.bfloat16)
    result = result.reshape(received.shape)
    returned = lax.all_to_all(result, "expert", split_axis=0, concat_axis=0, tiled=True)
    flat_out = returned.reshape(experts * capacity, model_width)
    picked = flat_out[flat_index].reshape(tok_dev, top_count, model_width)
    gates = gate_probs / jnp.sum(gate_probs, axis=1, keepdims=True)
    mixed_rows = jnp.einsum(
        "tk,tkd->td",
        gates,
        picked,
        preferred_element_type=jnp.float32,
        precision=lax.Precision.HIGHEST,
    )
    return (mixed_rows.astype(jnp.bfloat16), placed_gate_up, placed_down)


def solution(mesh):
    in_specs = (
        P(("dp", "expert"), None),
        P(("dp", "expert"), None),
        P(("dp", "expert"), None),
        P(),
        P("expert", None, "dp", None),
        P("expert", "dp", None),
    )
    out_specs = (P(("dp", "expert"), None), P("expert", None, "dp", None), P("expert", "dp", None))
    return jax.shard_map(
        per_device, mesh=mesh, in_specs=in_specs, out_specs=out_specs, check_vma=False
    )
```

```python
import jax
import jax.numpy as jnp
from jax import lax
from jax.sharding import PartitionSpec as P


def per_device(tokens, expert_ids, gate_probs, placement, w_gate_up, w_down):
    tok_dev = tokens.shape[0]
    model_width = tokens.shape[1]
    top_count = expert_ids.shape[1]
    experts = placement.shape[0]
    capacity = min(tok_dev, 3 * tok_dev * top_count // (2 * experts))
    slots = experts * capacity
    numbers = jnp.arange(experts, dtype=jnp.int32)

    gate_rows = w_gate_up.reshape(-1, model_width)
    down_rows = w_down.reshape(-1, model_width)
    shard = jnp.concatenate([gate_rows, down_rows], axis=0).reshape(experts, -1)
    spread = lax.all_to_all(shard, "expert", 0, 0, tiled=True)

    owner = (placement[None, None, :] == expert_ids[:, :, None]).astype(jnp.int32)
    old_ids = jnp.sum(owner * numbers[None, None, :], axis=2)
    choice = (old_ids[:, :, None] == numbers[None, None, :]).astype(jnp.float32)
    token_hot = jnp.sum(choice, axis=1)
    earlier = (
        jnp.arange(tok_dev, dtype=jnp.int32)[None, :] < jnp.arange(tok_dev, dtype=jnp.int32)[:, None]
    ).astype(jnp.float32)
    before = jnp.dot(earlier, token_hot, preferred_element_type=jnp.float32)
    slot_of = jnp.sum(before[:, None, :] * choice, axis=2).astype(jnp.int32)
    flat_index = old_ids * capacity + slot_of
    slot_numbers = jnp.arange(slots, dtype=jnp.int32)
    hits = flat_index[None, :, :] == slot_numbers[:, None, None]
    pick = jnp.any(hits, axis=2).astype(jnp.bfloat16)
    buffer = jnp.dot(pick, tokens, preferred_element_type=jnp.float32).astype(jnp.bfloat16)
    buffer = buffer.reshape(experts, capacity, model_width)
    spread, buffer = lax.optimization_barrier((spread, buffer))

    gathered = (
        lax.all_gather(w_gate_up, "dp", axis=2, tiled=True),
        lax.all_gather(w_down, "dp", axis=1, tiled=True),
    )
    hidden_count = gathered[0].shape[2]
    gate_up_full = gathered[0].reshape(2 * hidden_count, model_width)
    down_full = gathered[1].reshape(hidden_count, model_width)

    received = lax.all_to_all(buffer, "expert", split_axis=0, concat_axis=0, tiled=True)
    reordered = jnp.take(spread, jnp.sum(
        jnp.where(placement[:, None] == numbers[None, :], numbers[:, None], 0), axis=0
    ), axis=0)
    reordered, received = lax.optimization_barrier((reordered, received))
    placed_rows = lax.all_to_all(reordered, "expert", 0, 0, tiled=True)

    row_block = received.reshape(-1, model_width)
    projected = lax.dot_general(
        row_block, gate_up_full, (((1,), (1,)), ((), ())), preferred_element_type=jnp.float32
    )
    gate_part = projected[:, :hidden_count]
    up_part = projected[:, hidden_count:]
    hidden = (jax.nn.silu(gate_part) * up_part).astype(jnp.bfloat16)
    result = jnp.dot(hidden, down_full, preferred_element_type=jnp.float32).astype(jnp.bfloat16)
    result = result.reshape(received.shape)
    placed_rows, result = lax.optimization_barrier((placed_rows, result))
    returned = lax.all_to_all(result, "expert", split_axis=0, concat_axis=0, tiled=True)
    flat_out = returned.reshape(slots, model_width)

    placed_rows = placed_rows.reshape(-1, model_width)
    gate_count = gate_rows.shape[0]
    placed_gate_up = placed_rows[:gate_count].reshape(w_gate_up.shape)
    placed_down = placed_rows[gate_count:].reshape(w_down.shape)

    gates = gate_probs / jnp.sum(gate_probs, axis=1, keepdims=True)
    weights = jnp.sum(jnp.where(hits, gates[None, :, :], 0.0), axis=2).T
    weights_hi = weights.astype(jnp.bfloat16)
    weights_lo = (weights - weights_hi.astype(jnp.float32)).astype(jnp.bfloat16)
    mixed_rows = jnp.dot(weights_hi, flat_out, preferred_element_type=jnp.float32) + jnp.dot(
        weights_lo, flat_out, preferred_element_type=jnp.float32
    )
    return (mixed_rows.astype(jnp.bfloat16), placed_gate_up, placed_down)


def solution(mesh):
    in_specs = (
        P(("dp", "expert"), None),
        P(("dp", "expert"), None),
        P(("dp", "expert"), None),
        P(),
        P("expert", None, "dp", None),
        P("expert", "dp", None),
    )
    out_specs = (P(("dp", "expert"), None), P("expert", None, "dp", None), P("expert", "dp", None))
    return jax.shard_map(
        per_device, mesh=mesh, in_specs=in_specs, out_specs=out_specs, check_vma=False
    )
```

```python
import jax
import jax.numpy as jnp
from jax import lax
from jax.sharding import PartitionSpec as P


def per_device(tokens, expert_ids, gate_probs, placement, w_gate_up, w_down):
    tok_dev = tokens.shape[0]
    model_width = tokens.shape[1]
    top_count = expert_ids.shape[1]
    experts = placement.shape[0]
    capacity = min(tok_dev, 3 * tok_dev * top_count // (2 * experts))
    slots = experts * capacity
    numbers = jnp.arange(experts, dtype=jnp.int32)

    owner = (placement[None, None, :] == expert_ids[:, :, None]).astype(jnp.int32)
    old_ids = jnp.sum(owner * numbers[None, None, :], axis=2)
    choice = (old_ids[:, :, None] == numbers[None, None, :]).astype(jnp.float32)
    token_hot = jnp.sum(choice, axis=1)
    earlier = (
        jnp.arange(tok_dev, dtype=jnp.int32)[None, :] < jnp.arange(tok_dev, dtype=jnp.int32)[:, None]
    ).astype(jnp.float32)
    before = jnp.dot(earlier, token_hot, preferred_element_type=jnp.float32)
    slot_of = jnp.sum(before[:, None, :] * choice, axis=2).astype(jnp.int32)
    flat_index = old_ids * capacity + slot_of
    slot_numbers = jnp.arange(slots, dtype=jnp.int32)
    hits = flat_index[None, :, :] == slot_numbers[:, None, None]
    pick = jnp.any(hits, axis=2).astype(jnp.bfloat16)
    buffer = jnp.dot(pick, tokens, preferred_element_type=jnp.float32).astype(jnp.bfloat16)
    buffer = buffer.reshape(experts, capacity, model_width)

    gate_rows = w_gate_up.reshape(-1, model_width)
    down_rows = w_down.reshape(-1, model_width)
    shard = jnp.concatenate([gate_rows, down_rows], axis=0)
    chunks = shard.reshape(experts, capacity, -1)
    outgoing = jnp.concatenate([buffer, chunks], axis=2)

    gathered = (
        lax.all_gather(w_gate_up, "dp", axis=2, tiled=True),
        lax.all_gather(w_down, "dp", axis=1, tiled=True),
    )
    hidden_count = gathered[0].shape[2]
    gate_up_full = gathered[0].reshape(2 * hidden_count, model_width)
    down_full = gathered[1].reshape(hidden_count, model_width)

    arrived = lax.all_to_all(outgoing, "expert", split_axis=0, concat_axis=0, tiled=True)
    inverse = jnp.sum(jnp.where(placement[:, None] == numbers[None, :], numbers[:, None], 0), axis=0)
    reordered = jnp.take(arrived[:, :, model_width:], inverse, axis=0)

    row_block = arrived[:, :, :model_width].reshape(-1, model_width)
    projected = lax.dot_general(
        row_block, gate_up_full, (((1,), (1,)), ((), ())), preferred_element_type=jnp.float32
    )
    gate_part = projected[:, :hidden_count]
    up_part = projected[:, hidden_count:]
    hidden = (jax.nn.silu(gate_part) * up_part).astype(jnp.bfloat16)
    result = jnp.dot(hidden, down_full, preferred_element_type=jnp.float32).astype(jnp.bfloat16)
    result = result.reshape(experts, capacity, model_width)
    back = lax.all_to_all(
        jnp.concatenate([result, reordered], axis=2), "expert", split_axis=0, concat_axis=0, tiled=True
    )
    flat_out = back[:, :, :model_width].reshape(slots, model_width)

    placed_rows = back[:, :, model_width:].reshape(-1, model_width)
    gate_count = gate_rows.shape[0]
    placed_gate_up = placed_rows[:gate_count].reshape(w_gate_up.shape)
    placed_down = placed_rows[gate_count:].reshape(w_down.shape)

    gates = gate_probs / jnp.sum(gate_probs, axis=1, keepdims=True)
    weights = jnp.sum(jnp.where(hits, gates[None, :, :], 0.0), axis=2).T
    weights_hi = weights.astype(jnp.bfloat16)
    weights_lo = (weights - weights_hi.astype(jnp.float32)).astype(jnp.bfloat16)
    both = jnp.dot(
        jnp.concatenate([weights_hi, weights_lo], axis=0), flat_out, preferred_element_type=jnp.float32
    )
    mixed_rows = both[:tok_dev] + both[tok_dev:]
    return (mixed_rows.astype(jnp.bfloat16), placed_gate_up, placed_down)


def solution(mesh):
    in_specs = (
        P(("dp", "expert"), None),
        P(("dp", "expert"), None),
        P(("dp", "expert"), None),
        P(),
        P("expert", None, "dp", None),
        P("expert", "dp", None),
    )
    out_specs = (P(("dp", "expert"), None), P("expert", None, "dp", None), P("expert", "dp", None))
    return jax.shard_map(
        per_device, mesh=mesh, in_specs=in_specs, out_specs=out_specs, check_vma=False
    )
```

```python
import jax
import jax.numpy as jnp
from jax import lax
from jax.sharding import PartitionSpec as P


def per_device(tokens, expert_ids, gate_probs, placement, w_gate_up, w_down):
    tok_dev = tokens.shape[0]
    model_width = tokens.shape[1]
    top_count = expert_ids.shape[1]
    experts = placement.shape[0]
    capacity = min(tok_dev, 3 * tok_dev * top_count // (2 * experts))
    slots = experts * capacity
    numbers = jnp.arange(experts, dtype=jnp.int32)

    owner = (placement[None, None, :] == expert_ids[:, :, None]).astype(jnp.int32)
    old_ids = jnp.sum(owner * numbers[None, None, :], axis=2)
    choice = (old_ids[:, :, None] == numbers[None, None, :]).astype(jnp.float32)
    token_hot = jnp.sum(choice, axis=1)
    earlier = (
        jnp.arange(tok_dev, dtype=jnp.int32)[None, :] < jnp.arange(tok_dev, dtype=jnp.int32)[:, None]
    ).astype(jnp.float32)
    before = jnp.dot(earlier, token_hot, preferred_element_type=jnp.float32)
    slot_of = jnp.sum(before[:, None, :] * choice, axis=2).astype(jnp.int32)
    flat_index = old_ids * capacity + slot_of
    slot_numbers = jnp.arange(slots, dtype=jnp.int32)
    hits = flat_index.T[None, :, :] == slot_numbers[:, None, None]
    pick = jnp.any(hits, axis=1).astype(jnp.bfloat16).reshape(experts, capacity, tok_dev)
    head = 8 if capacity > 8 else capacity
    first_pick = pick[:, :head].reshape(-1, tok_dev)
    second_pick = pick[:, head:].reshape(-1, tok_dev)

    def select_rows(chosen):
        rows = jnp.dot(chosen, tokens, preferred_element_type=jnp.float32).astype(jnp.bfloat16)
        return rows.reshape(experts, -1, model_width)

    gate_rows = w_gate_up.reshape(experts, head, -1)
    down_rows = w_down.reshape(experts, head, -1)
    gate_width = gate_rows.shape[2]
    chunk_width = gate_width + down_rows.shape[2]

    gathered = (
        lax.all_gather(w_gate_up, "dp", axis=2, tiled=True),
        lax.all_gather(w_down, "dp", axis=1, tiled=True),
    )
    hidden_count = gathered[0].shape[2]
    gate_up_full = gathered[0].reshape(2 * hidden_count, model_width)
    down_full = gathered[1].reshape(hidden_count, model_width)

    def expert_block(rows):
        row_block = rows.reshape(-1, model_width)
        projected = lax.dot_general(
            row_block, gate_up_full, (((1,), (1,)), ((), ())), preferred_element_type=jnp.float32
        )
        gate_part = projected[:, :hidden_count]
        up_part = projected[:, hidden_count:]
        hidden = (jax.nn.silu(gate_part) * up_part).astype(jnp.bfloat16)
        out = jnp.dot(hidden, down_full, preferred_element_type=jnp.float32).astype(jnp.bfloat16)
        return out.reshape(experts, -1, model_width)

    def exchange(block):
        return lax.all_to_all(block, "expert", split_axis=0, concat_axis=0, tiled=True)

    first_out = jnp.concatenate([select_rows(first_pick), gate_rows, down_rows], axis=2)
    second_out = select_rows(second_pick)
    first_in = exchange(first_out)
    first_in, second_out = lax.optimization_barrier((first_in, second_out))
    second_in = exchange(second_out)

    inverse = jnp.sum(jnp.where(placement[:, None] == numbers[None, :], numbers[:, None], 0), axis=0)
    reordered = jnp.take(first_in[:, :, model_width:], inverse, axis=0)
    first_back = jnp.concatenate([expert_block(first_in[:, :, :model_width]), reordered], axis=2)
    second_in, first_back = lax.optimization_barrier((second_in, first_back))
    first_ret = exchange(first_back)
    second_back = expert_block(second_in)
    first_ret, second_back = lax.optimization_barrier((first_ret, second_back))
    second_ret = exchange(second_back)

    placed_chunks = first_ret[:, :, model_width:]
    placed_gate_up = placed_chunks[:, :, :gate_width].reshape(w_gate_up.shape)
    placed_down = placed_chunks[:, :, gate_width:chunk_width].reshape(w_down.shape)

    gates = gate_probs / jnp.sum(gate_probs, axis=1, keepdims=True)
    weights = jnp.sum(jnp.where(hits, gates.T[None, :, :], 0.0), axis=1)
    weights = weights.reshape(experts, capacity, tok_dev)

    def mix(part, returned):
        part = part.reshape(-1, tok_dev).T
        part_hi = part.astype(jnp.bfloat16)
        part_lo = (part - part_hi.astype(jnp.float32)).astype(jnp.bfloat16)
        flat = returned.reshape(-1, model_width)
        both = jnp.dot(
            jnp.concatenate([part_hi, part_lo], axis=0), flat, preferred_element_type=jnp.float32
        )
        return both[:tok_dev] + both[tok_dev:]

    mixed_rows = mix(weights[:, :head], first_ret[:, :, :model_width]) + mix(
        weights[:, head:], second_ret
    )
    return (mixed_rows.astype(jnp.bfloat16), placed_gate_up, placed_down)


def solution(mesh):
    in_specs = (
        P(("dp", "expert"), None),
        P(("dp", "expert"), None),
        P(("dp", "expert"), None),
        P(),
        P("expert", None, "dp", None),
        P("expert", "dp", None),
    )
    out_specs = (P(("dp", "expert"), None), P("expert", None, "dp", None), P("expert", "dp", None))
    return jax.shard_map(
        per_device, mesh=mesh, in_specs=in_specs, out_specs=out_specs, check_vma=False
    )
```

```python
import jax
import jax.numpy as jnp
from jax import lax
from jax.sharding import PartitionSpec as P


def per_device(tokens, expert_ids, gate_probs, placement, w_gate_up, w_down):
    tok_dev = tokens.shape[0]
    model_width = tokens.shape[1]
    top_count = expert_ids.shape[1]
    experts = placement.shape[0]
    capacity = min(tok_dev, 3 * tok_dev * top_count // (2 * experts))
    slots = experts * capacity
    numbers = jnp.arange(experts, dtype=jnp.int32)

    owner = (placement[None, None, :] == expert_ids[:, :, None]).astype(jnp.int32)
    old_ids = jnp.sum(owner * numbers[None, None, :], axis=2)
    choice = (old_ids[:, :, None] == numbers[None, None, :]).astype(jnp.float32)
    token_hot = jnp.sum(choice, axis=1)
    earlier = (
        jnp.arange(tok_dev, dtype=jnp.int32)[None, :] < jnp.arange(tok_dev, dtype=jnp.int32)[:, None]
    ).astype(jnp.float32)
    before = jnp.dot(earlier, token_hot, preferred_element_type=jnp.float32)
    slot_of = jnp.sum(before[:, None, :] * choice, axis=2).astype(jnp.int32)
    flat_index = old_ids * capacity + slot_of
    head = 8 if capacity > 8 else capacity
    slot_numbers = (
        numbers[:, None] * capacity + jnp.arange(capacity, dtype=jnp.int32)[None, :]
    )
    first_numbers = slot_numbers[:, :head].reshape(-1)
    second_numbers = slot_numbers[:, head:].reshape(-1)
    first_hits = flat_index.T[None, :, :] == first_numbers[:, None, None]
    second_hits = flat_index.T[None, :, :] == second_numbers[:, None, None]
    first_pick = jnp.any(first_hits, axis=1).astype(jnp.bfloat16)
    second_pick = jnp.any(second_hits, axis=1).astype(jnp.bfloat16)

    def select_rows(chosen):
        rows = jnp.dot(chosen, tokens, preferred_element_type=jnp.float32).astype(jnp.bfloat16)
        return rows.reshape(experts, -1, model_width)

    gate_rows = w_gate_up.reshape(experts, head, -1)
    down_rows = w_down.reshape(experts, head, -1)
    gate_width = gate_rows.shape[2]
    chunk_width = gate_width + down_rows.shape[2]

    gathered = (
        lax.all_gather(w_gate_up, "dp", axis=2, tiled=True),
        lax.all_gather(w_down, "dp", axis=1, tiled=True),
    )
    hidden_count = gathered[0].shape[2]
    gate_up_full = gathered[0].reshape(2 * hidden_count, model_width)
    down_full = gathered[1].reshape(hidden_count, model_width)

    def expert_block(rows):
        row_block = rows.reshape(-1, model_width)
        projected = lax.dot_general(
            row_block, gate_up_full, (((1,), (1,)), ((), ())), preferred_element_type=jnp.float32
        )
        gate_part = projected[:, :hidden_count]
        up_part = projected[:, hidden_count:]
        hidden = (jax.nn.silu(gate_part) * up_part).astype(jnp.bfloat16)
        out = jnp.dot(hidden, down_full, preferred_element_type=jnp.float32).astype(jnp.bfloat16)
        return out.reshape(experts, -1, model_width)

    def exchange(block):
        return lax.all_to_all(block, "expert", split_axis=0, concat_axis=0, tiled=True)

    first_out = jnp.concatenate([select_rows(first_pick), gate_rows, down_rows], axis=2)
    second_out = select_rows(second_pick)
    first_in = exchange(first_out)
    first_in, second_out = lax.optimization_barrier((first_in, second_out))
    second_in = exchange(second_out)

    inverse = jnp.sum(jnp.where(placement[:, None] == numbers[None, :], numbers[:, None], 0), axis=0)
    reordered = jnp.take(first_in[:, :, model_width:], inverse, axis=0)
    first_back = jnp.concatenate([expert_block(first_in[:, :, :model_width]), reordered], axis=2)
    second_in, first_back = lax.optimization_barrier((second_in, first_back))
    first_ret = exchange(first_back)
    second_back = expert_block(second_in)
    first_ret, second_back = lax.optimization_barrier((first_ret, second_back))
    second_ret = exchange(second_back)

    placed_chunks = first_ret[:, :, model_width:]
    placed_gate_up = placed_chunks[:, :, :gate_width].reshape(w_gate_up.shape)
    placed_down = placed_chunks[:, :, gate_width:chunk_width].reshape(w_down.shape)

    gates = gate_probs / jnp.sum(gate_probs, axis=1, keepdims=True)

    def mix(hits, returned):
        part = jnp.sum(jnp.where(hits, gates.T[None, :, :], 0.0), axis=1).T
        rounded = lax.reduce_precision(part, exponent_bits=8, mantissa_bits=7)
        part_hi = rounded.astype(jnp.bfloat16)
        part_lo = (part - rounded).astype(jnp.bfloat16)
        flat = returned.reshape(-1, model_width)
        both = jnp.dot(
            jnp.concatenate([part_hi, part_lo], axis=0), flat, preferred_element_type=jnp.float32
        )
        return both[:tok_dev] + both[tok_dev:]

    mixed_rows = mix(first_hits, first_ret[:, :, :model_width]) + mix(second_hits, second_ret)
    return (mixed_rows.astype(jnp.bfloat16), placed_gate_up, placed_down)


def solution(mesh):
    in_specs = (
        P(("dp", "expert"), None),
        P(("dp", "expert"), None),
        P(("dp", "expert"), None),
        P(),
        P("expert", None, "dp", None),
        P("expert", "dp", None),
    )
    out_specs = (P(("dp", "expert"), None), P("expert", None, "dp", None), P("expert", "dp", None))
    return jax.shard_map(
        per_device, mesh=mesh, in_specs=in_specs, out_specs=out_specs, check_vma=False
    )
```

```python
import jax
import jax.numpy as jnp
from jax import lax
from jax.sharding import PartitionSpec as P


def per_device(tokens, expert_ids, gate_probs, placement, w_gate_up, w_down):
    tok_dev = tokens.shape[0]
    model_width = tokens.shape[1]
    top_count = expert_ids.shape[1]
    experts = placement.shape[0]
    capacity = min(tok_dev, 3 * tok_dev * top_count // (2 * experts))
    slots = experts * capacity
    numbers = jnp.arange(experts, dtype=jnp.int32)

    owner = (placement[None, None, :] == expert_ids[:, :, None]).astype(jnp.int32)
    old_ids = jnp.sum(owner * numbers[None, None, :], axis=2)
    choice = (old_ids[:, :, None] == numbers[None, None, :]).astype(jnp.float32)
    token_hot = jnp.sum(choice, axis=1)
    earlier = (
        jnp.arange(tok_dev, dtype=jnp.int32)[None, :] < jnp.arange(tok_dev, dtype=jnp.int32)[:, None]
    ).astype(jnp.float32)
    before = jnp.dot(earlier, token_hot, preferred_element_type=jnp.float32)
    slot_of = jnp.sum(before[:, None, :] * choice, axis=2).astype(jnp.int32)
    flat_index = old_ids * capacity + slot_of
    head = 8 if capacity > 8 else capacity
    slot_numbers = (
        numbers[:, None] * capacity + jnp.arange(capacity, dtype=jnp.int32)[None, :]
    )
    first_numbers = slot_numbers[:, :head].reshape(-1)
    second_numbers = slot_numbers[:, head:].reshape(-1)
    first_hits = flat_index.T[None, :, :] == first_numbers[:, None, None]
    second_hits = flat_index.T[None, :, :] == second_numbers[:, None, None]
    first_pick = jnp.any(first_hits, axis=1).astype(jnp.bfloat16)
    second_pick = jnp.any(second_hits, axis=1).astype(jnp.bfloat16)

    def select_rows(chosen):
        rows = jnp.dot(chosen, tokens, preferred_element_type=jnp.float32).astype(jnp.bfloat16)
        return rows.reshape(experts, -1, model_width)

    gate_rows = w_gate_up.reshape(experts, head, -1)
    down_rows = w_down.reshape(experts, head, -1)
    gate_width = gate_rows.shape[2]
    chunk_width = gate_width + down_rows.shape[2]

    ring = lax.psum(1, "dp")
    own = jnp.concatenate(
        [w_gate_up.reshape(-1, model_width), w_down.reshape(-1, model_width)], axis=0
    )
    parts = [own] + [
        lax.ppermute(own, "dp", [(j, (j + shift) % ring) for j in range(ring)])
        for shift in range(1, ring)
    ]
    local_count = w_down.shape[1]
    hidden_count = local_count * ring
    gate_up_full = jnp.concatenate(
        [part[:local_count] for part in parts] + [part[local_count:2 * local_count] for part in parts],
        axis=0,
    )
    down_full = jnp.concatenate([part[2 * local_count:] for part in parts], axis=0)

    def expert_block(rows):
        row_block = rows.reshape(-1, model_width)
        projected = lax.dot_general(
            row_block, gate_up_full, (((1,), (1,)), ((), ())), preferred_element_type=jnp.float32
        )
        gate_part = projected[:, :hidden_count]
        up_part = projected[:, hidden_count:]
        hidden = (jax.nn.silu(gate_part) * up_part).astype(jnp.bfloat16)
        out = jnp.dot(hidden, down_full, preferred_element_type=jnp.float32).astype(jnp.bfloat16)
        return out.reshape(experts, -1, model_width)

    def exchange(block):
        return lax.all_to_all(block, "expert", split_axis=0, concat_axis=0, tiled=True)

    first_out = jnp.concatenate([select_rows(first_pick), gate_rows, down_rows], axis=2)
    second_out = select_rows(second_pick)
    first_in = exchange(first_out)
    first_in, second_out = lax.optimization_barrier((first_in, second_out))
    second_in = exchange(second_out)

    inverse = jnp.sum(jnp.where(placement[:, None] == numbers[None, :], numbers[:, None], 0), axis=0)
    reordered = jnp.take(first_in[:, :, model_width:], inverse, axis=0)
    first_back = jnp.concatenate([expert_block(first_in[:, :, :model_width]), reordered], axis=2)
    second_in, first_back = lax.optimization_barrier((second_in, first_back))
    first_ret = exchange(first_back)
    second_back = expert_block(second_in)
    first_ret, second_back = lax.optimization_barrier((first_ret, second_back))
    second_ret = exchange(second_back)

    placed_chunks = first_ret[:, :, model_width:]
    placed_gate_up = placed_chunks[:, :, :gate_width].reshape(w_gate_up.shape)
    placed_down = placed_chunks[:, :, gate_width:chunk_width].reshape(w_down.shape)

    gates = gate_probs / jnp.sum(gate_probs, axis=1, keepdims=True)

    def mix(hits, returned):
        part = jnp.sum(jnp.where(hits, gates.T[None, :, :], 0.0), axis=1).T
        rounded = lax.reduce_precision(part, exponent_bits=8, mantissa_bits=7)
        part_hi = rounded.astype(jnp.bfloat16)
        part_lo = (part - rounded).astype(jnp.bfloat16)
        flat = returned.reshape(-1, model_width)
        both = jnp.dot(
            jnp.concatenate([part_hi, part_lo], axis=0), flat, preferred_element_type=jnp.float32
        )
        return both[:tok_dev] + both[tok_dev:]

    mixed_rows = mix(first_hits, first_ret[:, :, :model_width]) + mix(second_hits, second_ret)
    return (mixed_rows.astype(jnp.bfloat16), placed_gate_up, placed_down)


def solution(mesh):
    in_specs = (
        P(("dp", "expert"), None),
        P(("dp", "expert"), None),
        P(("dp", "expert"), None),
        P(),
        P("expert", None, "dp", None),
        P("expert", "dp", None),
    )
    out_specs = (P(("dp", "expert"), None), P("expert", None, "dp", None), P("expert", "dp", None))
    return jax.shard_map(
        per_device, mesh=mesh, in_specs=in_specs, out_specs=out_specs, check_vma=False
    )
```

```python
import jax
import jax.numpy as jnp
from jax import lax
from jax.sharding import PartitionSpec as P


def per_device(tokens, expert_ids, gate_probs, placement, w_gate_up, w_down):
    tok_dev = tokens.shape[0]
    model_width = tokens.shape[1]
    top_count = expert_ids.shape[1]
    experts = placement.shape[0]
    capacity = min(tok_dev, 3 * tok_dev * top_count // (2 * experts))
    slots = experts * capacity
    numbers = jnp.arange(experts, dtype=jnp.int32)

    owner = (placement[None, None, :] == expert_ids[:, :, None]).astype(jnp.int32)
    old_ids = jnp.sum(owner * numbers[None, None, :], axis=2)
    choice = (old_ids[:, :, None] == numbers[None, None, :]).astype(jnp.float32)
    token_hot = jnp.sum(choice, axis=1)
    earlier = (
        jnp.arange(tok_dev, dtype=jnp.int32)[None, :] < jnp.arange(tok_dev, dtype=jnp.int32)[:, None]
    ).astype(jnp.float32)
    before = jnp.dot(earlier, token_hot, preferred_element_type=jnp.float32)
    slot_of = jnp.sum(before[:, None, :] * choice, axis=2).astype(jnp.int32)
    flat_index = old_ids * capacity + slot_of
    slot_numbers = jnp.arange(slots, dtype=jnp.int32)
    hits = flat_index.T[None, :, :] == slot_numbers[:, None, None]
    pick = jnp.any(hits, axis=1).astype(jnp.bfloat16)

    def exchange(block):
        return lax.all_to_all(block, "expert", split_axis=0, concat_axis=0, tiled=True)

    gate_rows = w_gate_up.reshape(-1, model_width)
    down_rows = w_down.reshape(-1, model_width)
    shard = jnp.concatenate([gate_rows, down_rows], axis=0)
    spread = exchange(shard.reshape(experts, capacity, -1))

    ring = lax.psum(1, "dp")
    parts = [shard] + [
        lax.ppermute(shard, "dp", [(j, (j + shift) % ring) for j in range(ring)])
        for shift in range(1, ring)
    ]
    local_count = w_down.shape[1]
    hidden_count = local_count * ring
    gate_up_full = jnp.concatenate(
        [part[:local_count] for part in parts] + [part[local_count:2 * local_count] for part in parts],
        axis=0,
    )
    down_full = jnp.concatenate([part[2 * local_count:] for part in parts], axis=0)

    buffer = jnp.dot(pick, tokens, preferred_element_type=jnp.float32).astype(jnp.bfloat16)
    buffer = buffer.reshape(experts, capacity, model_width)
    spread, buffer = lax.optimization_barrier((spread, buffer))
    received = exchange(buffer)

    inverse = jnp.sum(jnp.where(placement[:, None] == numbers[None, :], numbers[:, None], 0), axis=0)
    reordered = jnp.take(spread, inverse, axis=0, mode="clip")
    received, reordered = lax.optimization_barrier((received, reordered))
    placed_rows = exchange(reordered)

    row_block = received.reshape(-1, model_width)
    projected = lax.dot_general(
        row_block, gate_up_full, (((1,), (1,)), ((), ())), preferred_element_type=jnp.float32
    )
    gate_part = projected[:, :hidden_count]
    up_part = projected[:, hidden_count:]
    hidden = (jax.nn.silu(gate_part) * up_part).astype(jnp.bfloat16)
    result = jnp.dot(hidden, down_full, preferred_element_type=jnp.float32).astype(jnp.bfloat16)
    result = result.reshape(experts, capacity, model_width)
    placed_rows, result = lax.optimization_barrier((placed_rows, result))
    returned = exchange(result)

    placed_rows = placed_rows.reshape(-1, model_width)
    gate_count = gate_rows.shape[0]
    placed_gate_up = placed_rows[:gate_count].reshape(w_gate_up.shape)
    placed_down = placed_rows[gate_count:].reshape(w_down.shape)

    gates = gate_probs / jnp.sum(gate_probs, axis=1, keepdims=True)
    part = jnp.sum(jnp.where(hits, gates.T[None, :, :], 0.0), axis=1).T
    rounded = lax.reduce_precision(part, exponent_bits=8, mantissa_bits=7)
    part_hi = rounded.astype(jnp.bfloat16)
    part_lo = (part - rounded).astype(jnp.bfloat16)
    both = jnp.dot(
        jnp.concatenate([part_hi, part_lo], axis=0),
        returned.reshape(slots, model_width),
        preferred_element_type=jnp.float32,
    )
    mixed_rows = both[:tok_dev] + both[tok_dev:]
    return (mixed_rows.astype(jnp.bfloat16), placed_gate_up, placed_down)


def solution(mesh):
    in_specs = (
        P(("dp", "expert"), None),
        P(("dp", "expert"), None),
        P(("dp", "expert"), None),
        P(),
        P("expert", None, "dp", None),
        P("expert", "dp", None),
    )
    out_specs = (P(("dp", "expert"), None), P("expert", None, "dp", None), P("expert", "dp", None))
    return jax.shard_map(
        per_device, mesh=mesh, in_specs=in_specs, out_specs=out_specs, check_vma=False
    )
```

```python
import jax
import jax.numpy as jnp
from jax import lax
from jax.sharding import PartitionSpec as P


def per_device(tokens, expert_ids, gate_probs, placement, w_gate_up, w_down):
    tok_dev = tokens.shape[0]
    model_width = tokens.shape[1]
    top_count = expert_ids.shape[1]
    experts = placement.shape[0]
    capacity = min(tok_dev, 3 * tok_dev * top_count // (2 * experts))
    slots = experts * capacity
    numbers = jnp.arange(experts, dtype=jnp.int32)

    owner = (placement[None, None, :] == expert_ids[:, :, None]).astype(jnp.int32)
    old_ids = jnp.sum(owner * numbers[None, None, :], axis=2)
    choice = (old_ids[:, :, None] == numbers[None, None, :]).astype(jnp.float32)
    token_hot = jnp.sum(choice, axis=1)
    earlier = (
        jnp.arange(tok_dev, dtype=jnp.int32)[None, :] < jnp.arange(tok_dev, dtype=jnp.int32)[:, None]
    ).astype(jnp.float32)
    before = jnp.dot(earlier, token_hot, preferred_element_type=jnp.float32)
    slot_of = jnp.sum(before[:, None, :] * choice, axis=2).astype(jnp.int32)
    flat_index = old_ids * capacity + slot_of
    slot_numbers = jnp.arange(slots, dtype=jnp.int32)
    hits = flat_index.T[None, :, :] == slot_numbers[:, None, None]
    pick = jnp.any(hits, axis=1).astype(jnp.bfloat16)

    def exchange(block):
        return lax.all_to_all(block, "expert", split_axis=0, concat_axis=0, tiled=True)

    gate_rows = w_gate_up.reshape(-1, model_width)
    down_rows = w_down.reshape(-1, model_width)
    shard = jnp.concatenate([gate_rows, down_rows], axis=0)
    spread = exchange(shard.reshape(experts, capacity, -1))

    ring = lax.psum(1, "dp")
    parts = [shard] + [
        lax.ppermute(shard, "dp", [(j, (j + shift) % ring) for j in range(ring)])
        for shift in range(1, ring)
    ]
    local_count = w_down.shape[1]
    hidden_count = local_count * ring
    gate_up_full = jnp.concatenate(
        [part[:local_count] for part in parts] + [part[local_count:2 * local_count] for part in parts],
        axis=0,
    )
    down_full = jnp.concatenate([part[2 * local_count:] for part in parts], axis=0)

    buffer = jnp.dot(pick, tokens, preferred_element_type=jnp.float32).astype(jnp.bfloat16)
    buffer = buffer.reshape(experts, capacity, model_width)
    spread, buffer = lax.optimization_barrier((spread, buffer))
    received = exchange(buffer)

    inverse = jnp.sum(jnp.where(placement[:, None] == numbers[None, :], numbers[:, None], 0), axis=0)
    reordered = jnp.take(spread, inverse, axis=0, mode="clip")
    received, reordered = lax.optimization_barrier((received, reordered))
    placed_rows = exchange(reordered)

    row_block = received.reshape(-1, model_width)
    projected = lax.dot_general(
        row_block, gate_up_full, (((1,), (1,)), ((), ())), preferred_element_type=jnp.float32
    )
    gate_part = projected[:, :hidden_count]
    up_part = projected[:, hidden_count:]
    hidden = (jax.nn.silu(gate_part) * up_part).astype(jnp.bfloat16)
    result = jnp.dot(hidden, down_full, preferred_element_type=jnp.float32).astype(jnp.bfloat16)
    result = result.reshape(experts, capacity, model_width)
    placed_rows, result = lax.optimization_barrier((placed_rows, result))
    returned = exchange(result)

    placed_rows = placed_rows.reshape(-1, model_width)
    gate_count = gate_rows.shape[0]
    placed_gate_up = placed_rows[:gate_count].reshape(w_gate_up.shape)
    placed_down = placed_rows[gate_count:].reshape(w_down.shape)

    gates = gate_probs / jnp.sum(gate_probs, axis=1, keepdims=True)
    part = jnp.sum(jnp.where(hits, gates.T[None, :, :], 0.0), axis=1).T
    rounded = lax.reduce_precision(part, exponent_bits=8, mantissa_bits=7)
    part_hi = rounded.astype(jnp.bfloat16)
    part_lo = (part - rounded).astype(jnp.bfloat16)
    both = lax.dot_general(
        returned.reshape(slots, model_width),
        jnp.concatenate([part_hi, part_lo], axis=0),
        (((0,), (1,)), ((), ())),
        preferred_element_type=jnp.float32,
    )
    mixed_rows = (both[:, :tok_dev] + both[:, tok_dev:]).T
    return (mixed_rows.astype(jnp.bfloat16), placed_gate_up, placed_down)


def solution(mesh):
    in_specs = (
        P(("dp", "expert"), None),
        P(("dp", "expert"), None),
        P(("dp", "expert"), None),
        P(),
        P("expert", None, "dp", None),
        P("expert", "dp", None),
    )
    out_specs = (P(("dp", "expert"), None), P("expert", None, "dp", None), P("expert", "dp", None))
    return jax.shard_map(
        per_device, mesh=mesh, in_specs=in_specs, out_specs=out_specs, check_vma=False
    )
```

```python
import jax
import jax.numpy as jnp
from jax import lax
from jax.sharding import PartitionSpec as P


def per_device(tokens, expert_ids, gate_probs, placement, w_gate_up, w_down):
    tok_dev = tokens.shape[0]
    model_width = tokens.shape[1]
    top_count = expert_ids.shape[1]
    experts = placement.shape[0]
    capacity = min(tok_dev, 3 * tok_dev * top_count // (2 * experts))
    slots = experts * capacity
    numbers = jnp.arange(experts, dtype=jnp.int32)

    owner = (placement[None, None, :] == expert_ids[:, :, None]).astype(jnp.int32)
    old_ids = jnp.sum(owner * numbers[None, None, :], axis=2)
    choice = (old_ids[:, :, None] == numbers[None, None, :]).astype(jnp.float32)
    token_hot = jnp.sum(choice, axis=1)
    earlier = (
        jnp.arange(tok_dev, dtype=jnp.int32)[None, :] < jnp.arange(tok_dev, dtype=jnp.int32)[:, None]
    ).astype(jnp.float32)
    before = jnp.dot(earlier, token_hot, preferred_element_type=jnp.float32)
    slot_of = jnp.sum(before[:, None, :] * choice, axis=2).astype(jnp.int32)
    flat_index = old_ids * capacity + slot_of
    slot_numbers = jnp.arange(slots, dtype=jnp.int32)
    hits = flat_index.T[None, :, :] == slot_numbers[:, None, None]
    pick = jnp.any(hits, axis=1).astype(jnp.bfloat16)

    def exchange(block):
        return lax.all_to_all(block, "expert", split_axis=0, concat_axis=0, tiled=True)

    gate_rows = w_gate_up.reshape(-1, model_width)
    down_rows = w_down.reshape(-1, model_width)
    shard = jnp.concatenate([gate_rows, down_rows], axis=0)
    spread = exchange(shard.reshape(experts, capacity, -1))

    ring = lax.psum(1, "dp")
    parts = [shard] + [
        lax.ppermute(shard, "dp", [(j, (j + shift) % ring) for j in range(ring)])
        for shift in range(1, ring)
    ]
    local_count = w_down.shape[1]
    hidden_count = local_count * ring
    gate_up_full = jnp.concatenate(
        [part[:local_count] for part in parts] + [part[local_count:2 * local_count] for part in parts],
        axis=0,
    )
    down_full = jnp.concatenate([part[2 * local_count:] for part in parts], axis=0)

    buffer = jnp.dot(pick, tokens, preferred_element_type=jnp.float32).astype(jnp.bfloat16)
    buffer = buffer.reshape(experts, capacity, model_width)
    spread, buffer = lax.optimization_barrier((spread, buffer))
    received = exchange(buffer)

    inverse = jnp.sum(jnp.where(placement[:, None] == numbers[None, :], numbers[:, None], 0), axis=0)
    reordered = jnp.take(spread, inverse, axis=0, mode="clip")
    received, reordered = lax.optimization_barrier((received, reordered))
    placed_rows = exchange(reordered)

    row_block = received.reshape(-1, model_width)
    projected = lax.dot_general(
        row_block, gate_up_full, (((1,), (1,)), ((), ())), preferred_element_type=jnp.float32
    )
    gate_part = projected[:, :hidden_count]
    up_part = projected[:, hidden_count:]
    hidden = (jax.nn.silu(gate_part) * up_part).astype(jnp.bfloat16)
    result = jnp.dot(hidden, down_full, preferred_element_type=jnp.float32).astype(jnp.bfloat16)
    result = result.reshape(experts, capacity, model_width)
    placed_rows, result = lax.optimization_barrier((placed_rows, result))
    returned = exchange(result)

    placed_rows = placed_rows.reshape(-1, model_width)
    gate_count = gate_rows.shape[0]
    placed_gate_up = placed_rows[:gate_count].reshape(w_gate_up.shape)
    placed_down = placed_rows[gate_count:].reshape(w_down.shape)

    gates = gate_probs / jnp.sum(gate_probs, axis=1, keepdims=True)
    part = jnp.sum(jnp.where(hits, gates.T[None, :, :], 0.0), axis=1).T
    mixed_rows = jnp.dot(
        part.astype(jnp.bfloat16), returned.reshape(slots, model_width), preferred_element_type=jnp.float32
    )
    return (mixed_rows.astype(jnp.bfloat16), placed_gate_up, placed_down)


def solution(mesh):
    in_specs = (
        P(("dp", "expert"), None),
        P(("dp", "expert"), None),
        P(("dp", "expert"), None),
        P(),
        P("expert", None, "dp", None),
        P("expert", "dp", None),
    )
    out_specs = (P(("dp", "expert"), None), P("expert", None, "dp", None), P("expert", "dp", None))
    return jax.shard_map(
        per_device, mesh=mesh, in_specs=in_specs, out_specs=out_specs, check_vma=False
    )
```

```python
import jax
import jax.numpy as jnp
from jax import lax
from jax.sharding import PartitionSpec as P


def per_device(tokens, expert_ids, gate_probs, placement, w_gate_up, w_down):
    tok_dev = tokens.shape[0]
    model_width = tokens.shape[1]
    top_count = expert_ids.shape[1]
    experts = placement.shape[0]
    capacity = min(tok_dev, 3 * tok_dev * top_count // (2 * experts))
    slots = experts * capacity
    numbers = jnp.arange(experts, dtype=jnp.int32)

    owner = (placement[None, None, :] == expert_ids[:, :, None]).astype(jnp.int32)
    old_ids = jnp.sum(owner * numbers[None, None, :], axis=2)
    choice = (old_ids[:, :, None] == numbers[None, None, :]).astype(jnp.float32)
    token_hot = jnp.sum(choice, axis=1)
    earlier = (
        jnp.arange(tok_dev, dtype=jnp.int32)[None, :] < jnp.arange(tok_dev, dtype=jnp.int32)[:, None]
    ).astype(jnp.float32)
    before = jnp.dot(earlier, token_hot, preferred_element_type=jnp.float32)
    slot_of = jnp.sum(before[:, None, :] * choice, axis=2).astype(jnp.int32)
    flat_index = old_ids * capacity + slot_of
    slot_numbers = jnp.arange(slots, dtype=jnp.int32)
    hits = flat_index.T[None, :, :] == slot_numbers[:, None, None]
    pick = jnp.any(hits, axis=1).astype(jnp.bfloat16)

    def exchange(block):
        return lax.all_to_all(block, "expert", split_axis=0, concat_axis=0, tiled=True)

    gate_rows = w_gate_up.reshape(-1, model_width)
    down_rows = w_down.reshape(-1, model_width)
    shard = jnp.concatenate([gate_rows, down_rows], axis=0)
    sub, lane = 8, 128
    tiled = shard.reshape(shard.shape[0] // sub, sub, model_width // lane, lane).transpose(0, 2, 1, 3)
    spread = exchange(tiled.reshape(experts, -1, sub, lane))

    ring = lax.psum(1, "dp")
    parts = [shard] + [
        lax.ppermute(shard, "dp", [(j, (j + shift) % ring) for j in range(ring)])
        for shift in range(1, ring)
    ]
    local_count = w_down.shape[1]
    hidden_count = local_count * ring
    gate_up_full = jnp.concatenate(
        [part[:local_count] for part in parts] + [part[local_count:2 * local_count] for part in parts],
        axis=0,
    )
    down_full = jnp.concatenate([part[2 * local_count:] for part in parts], axis=0)

    buffer = jnp.dot(pick, tokens, preferred_element_type=jnp.float32).astype(jnp.bfloat16)
    buffer = buffer.reshape(experts, capacity, model_width)
    spread, buffer = lax.optimization_barrier((spread, buffer))
    received = exchange(buffer)

    inverse = jnp.sum(jnp.where(placement[:, None] == numbers[None, :], numbers[:, None], 0), axis=0)
    reordered = jnp.take(spread, inverse, axis=0, mode="clip")
    received, reordered = lax.optimization_barrier((received, reordered))
    placed_rows = exchange(reordered)

    row_block = received.reshape(-1, model_width)
    projected = lax.dot_general(
        row_block, gate_up_full, (((1,), (1,)), ((), ())), preferred_element_type=jnp.float32
    )
    gate_part = projected[:, :hidden_count]
    up_part = projected[:, hidden_count:]
    hidden = (jax.nn.silu(gate_part) * up_part).astype(jnp.bfloat16)
    result = jnp.dot(hidden, down_full, preferred_element_type=jnp.float32).astype(jnp.bfloat16)
    result = result.reshape(experts, capacity, model_width)
    placed_rows, result = lax.optimization_barrier((placed_rows, result))
    returned = exchange(result)

    placed_rows = placed_rows.reshape(tiled.shape).transpose(0, 2, 1, 3).reshape(-1, model_width)
    gate_count = gate_rows.shape[0]
    placed_gate_up = placed_rows[:gate_count].reshape(w_gate_up.shape)
    placed_down = placed_rows[gate_count:].reshape(w_down.shape)

    gates = gate_probs / jnp.sum(gate_probs, axis=1, keepdims=True)
    part = jnp.sum(jnp.where(hits, gates.T[None, :, :], 0.0), axis=1).T
    rounded = lax.reduce_precision(part, exponent_bits=8, mantissa_bits=7)
    part_hi = rounded.astype(jnp.bfloat16)
    part_lo = (part - rounded).astype(jnp.bfloat16)
    both = jnp.dot(
        jnp.concatenate([part_hi, part_lo], axis=0),
        returned.reshape(slots, model_width),
        preferred_element_type=jnp.float32,
    )
    mixed_rows = both[:tok_dev] + both[tok_dev:]
    return (mixed_rows.astype(jnp.bfloat16), placed_gate_up, placed_down)


def solution(mesh):
    in_specs = (
        P(("dp", "expert"), None),
        P(("dp", "expert"), None),
        P(("dp", "expert"), None),
        P(),
        P("expert", None, "dp", None),
        P("expert", "dp", None),
    )
    out_specs = (P(("dp", "expert"), None), P("expert", None, "dp", None), P("expert", "dp", None))
    return jax.shard_map(
        per_device, mesh=mesh, in_specs=in_specs, out_specs=out_specs, check_vma=False
    )
```

```python
import jax
import jax.numpy as jnp
from jax import lax
from jax.sharding import PartitionSpec as P
from jax.experimental import pallas as pl
from jax.experimental.pallas import tpu as pltpu


def per_device(tokens, expert_ids, gate_probs, placement, w_gate_up, w_down):
    tok_dev = tokens.shape[0]
    model_width = tokens.shape[1]
    top_count = expert_ids.shape[1]
    experts = placement.shape[0]
    capacity = min(tok_dev, 3 * tok_dev * top_count // (2 * experts))
    slots = experts * capacity
    numbers = jnp.arange(experts, dtype=jnp.int32)

    owner = (placement[None, None, :] == expert_ids[:, :, None]).astype(jnp.int32)
    old_ids = jnp.sum(owner * numbers[None, None, :], axis=2)
    choice = (old_ids[:, :, None] == numbers[None, None, :]).astype(jnp.float32)
    token_hot = jnp.sum(choice, axis=1)
    earlier = (
        jnp.arange(tok_dev, dtype=jnp.int32)[None, :] < jnp.arange(tok_dev, dtype=jnp.int32)[:, None]
    ).astype(jnp.float32)
    before = jnp.dot(earlier, token_hot, preferred_element_type=jnp.float32)
    slot_of = jnp.sum(before[:, None, :] * choice, axis=2).astype(jnp.int32)
    flat_index = old_ids * capacity + slot_of
    slot_numbers = jnp.arange(slots, dtype=jnp.int32)
    hits = flat_index.T[None, :, :] == slot_numbers[:, None, None]
    pick = jnp.any(hits, axis=1).astype(jnp.bfloat16)

    def exchange(block):
        return lax.all_to_all(block, "expert", split_axis=0, concat_axis=0, tiled=True)

    gate_rows = w_gate_up.reshape(-1, model_width)
    down_rows = w_down.reshape(-1, model_width)
    shard = jnp.concatenate([gate_rows, down_rows], axis=0)
    sub, lane = 8, 128
    tiled = shard.reshape(shard.shape[0] // sub, sub, model_width // lane, lane).transpose(0, 2, 1, 3)
    spread = exchange(tiled.reshape(experts, -1, sub, lane))

    ring = lax.psum(1, "dp")
    parts = [shard] + [
        lax.ppermute(shard, "dp", [(j, (j + shift) % ring) for j in range(ring)])
        for shift in range(1, ring)
    ]
    local_count = w_down.shape[1]
    hidden_count = local_count * ring
    gate_up_full = jnp.concatenate(
        [part[:local_count] for part in parts] + [part[local_count:2 * local_count] for part in parts],
        axis=0,
    )
    down_full = jnp.concatenate([part[2 * local_count:] for part in parts], axis=0)

    buffer = jnp.dot(pick, tokens, preferred_element_type=jnp.float32).astype(jnp.bfloat16)
    buffer = buffer.reshape(experts, capacity, model_width)
    spread, buffer = lax.optimization_barrier((spread, buffer))
    received = exchange(buffer)

    inverse = jnp.sum(jnp.where(placement[:, None] == numbers[None, :], numbers[:, None], 0), axis=0)
    reordered = jnp.take(spread, inverse, axis=0, mode="clip")
    received, reordered = lax.optimization_barrier((received, reordered))
    placed_rows = exchange(reordered)

    row_block = received.reshape(-1, model_width)
    projected = lax.dot_general(
        row_block, gate_up_full, (((1,), (1,)), ((), ())), preferred_element_type=jnp.float32
    )
    gate_part = projected[:, :hidden_count]
    up_part = projected[:, hidden_count:]
    hidden = (jax.nn.silu(gate_part) * up_part).astype(jnp.bfloat16)
    result = jnp.dot(hidden, down_full, preferred_element_type=jnp.float32).astype(jnp.bfloat16)
    result = result.reshape(experts, capacity, model_width)
    placed_rows, result = lax.optimization_barrier((placed_rows, result))
    returned = exchange(result)

    placed_rows = placed_rows.reshape(tiled.shape).transpose(0, 2, 1, 3).reshape(-1, model_width)
    gate_count = gate_rows.shape[0]
    placed_gate_up = placed_rows[:gate_count].reshape(w_gate_up.shape)
    placed_down = placed_rows[gate_count:].reshape(w_down.shape)

    gates = gate_probs / jnp.sum(gate_probs, axis=1, keepdims=True)
    part = jnp.sum(jnp.where(hits, gates.T[None, :, :], 0.0), axis=1).T
    rounded = lax.reduce_precision(part, exponent_bits=8, mantissa_bits=7)
    part_hi = rounded.astype(jnp.bfloat16)
    part_lo = (part - rounded).astype(jnp.bfloat16)
    mixed_rows = combine(part_hi, part_lo, returned.reshape(slots, model_width))
    return (mixed_rows, placed_gate_up, placed_down)


def combine_kernel(hi_ref, lo_ref, rows_ref, out_ref):
    rows = rows_ref[...]
    total = jnp.dot(hi_ref[...], rows, preferred_element_type=jnp.float32)
    total = total + jnp.dot(lo_ref[...], rows, preferred_element_type=jnp.float32)
    out_ref[...] = total.astype(out_ref.dtype)


def combine(hi, lo, rows):
    count, depth = hi.shape
    width = rows.shape[1]
    block = 512
    return pl.pallas_call(
        combine_kernel,
        out_shape=jax.ShapeDtypeStruct((count, width), jnp.bfloat16),
        grid=(width // block,),
        in_specs=[
            pl.BlockSpec((count, depth), lambda j: (0, 0)),
            pl.BlockSpec((count, depth), lambda j: (0, 0)),
            pl.BlockSpec((depth, block), lambda j: (0, j)),
        ],
        out_specs=pl.BlockSpec((count, block), lambda j: (0, j)),
        cost_estimate=pl.CostEstimate(
            flops=4 * count * depth * width,
            bytes_accessed=2 * (2 * count * depth + depth * width + count * width),
            transcendentals=0,
        ),
    )(hi, lo, rows)


def solution(mesh):
    in_specs = (
        P(("dp", "expert"), None),
        P(("dp", "expert"), None),
        P(("dp", "expert"), None),
        P(),
        P("expert", None, "dp", None),
        P("expert", "dp", None),
    )
    out_specs = (P(("dp", "expert"), None), P("expert", None, "dp", None), P("expert", "dp", None))
    return jax.shard_map(
        per_device, mesh=mesh, in_specs=in_specs, out_specs=out_specs, check_vma=False
    )
```

```python
import jax
import jax.numpy as jnp
from jax import lax
from jax.sharding import PartitionSpec as P


def per_device(tokens, expert_ids, gate_probs, placement, w_gate_up, w_down):
    tok_dev = tokens.shape[0]
    model_width = tokens.shape[1]
    top_count = expert_ids.shape[1]
    experts = placement.shape[0]
    capacity = min(tok_dev, 3 * tok_dev * top_count // (2 * experts))
    slots = experts * capacity
    numbers = jnp.arange(experts, dtype=jnp.int32)

    owner = (placement[None, None, :] == expert_ids[:, :, None]).astype(jnp.int32)
    old_ids = jnp.sum(owner * numbers[None, None, :], axis=2)
    choice = (old_ids[:, :, None] == numbers[None, None, :]).astype(jnp.float32)
    token_hot = jnp.sum(choice, axis=1)
    earlier = (
        jnp.arange(tok_dev, dtype=jnp.int32)[None, :] < jnp.arange(tok_dev, dtype=jnp.int32)[:, None]
    ).astype(jnp.float32)
    before = jnp.dot(earlier, token_hot, preferred_element_type=jnp.float32)
    slot_of = jnp.sum(before[:, None, :] * choice, axis=2).astype(jnp.int32)
    flat_index = old_ids * capacity + slot_of
    slot_numbers = jnp.arange(slots, dtype=jnp.int32)
    hits = flat_index.T[None, :, :] == slot_numbers[:, None, None]
    pick = jnp.any(hits, axis=1).astype(jnp.bfloat16)

    def exchange(block):
        return lax.all_to_all(block, "expert", split_axis=0, concat_axis=0, tiled=True)

    gate_rows = w_gate_up.reshape(-1, model_width)
    down_rows = w_down.reshape(-1, model_width)
    shard = jnp.concatenate([gate_rows, down_rows], axis=0)
    sub, lane = 8, 128
    tiled = shard.reshape(shard.shape[0] // sub, sub, model_width // lane, lane).transpose(0, 2, 1, 3)
    spread = exchange(tiled.reshape(experts, -1, sub, lane))

    ring = lax.psum(1, "dp")
    parts = [shard] + [
        lax.ppermute(shard, "dp", [(j, (j + shift) % ring) for j in range(ring)])
        for shift in range(1, ring)
    ]
    buffer = jnp.dot(pick, tokens, preferred_element_type=jnp.float32).astype(jnp.bfloat16)
    buffer = buffer.reshape(experts, capacity, model_width)
    spread, buffer, parts[1] = lax.optimization_barrier((spread, buffer, parts[1]))
    received = exchange(buffer)
    local_count = w_down.shape[1]
    hidden_count = local_count * ring
    gate_up_full = jnp.concatenate(
        [part[:local_count] for part in parts] + [part[local_count:2 * local_count] for part in parts],
        axis=0,
    )
    down_full = jnp.concatenate([part[2 * local_count:] for part in parts], axis=0)


    inverse = jnp.sum(jnp.where(placement[:, None] == numbers[None, :], numbers[:, None], 0), axis=0)
    reordered = jnp.take(spread, inverse, axis=0, mode="clip")
    received, reordered = lax.optimization_barrier((received, reordered))
    placed_rows = exchange(reordered)

    row_block = received.reshape(-1, model_width)
    projected = lax.dot_general(
        row_block, gate_up_full, (((1,), (1,)), ((), ())), preferred_element_type=jnp.float32
    )
    gate_part = projected[:, :hidden_count]
    up_part = projected[:, hidden_count:]
    hidden = (jax.nn.silu(gate_part) * up_part).astype(jnp.bfloat16)
    result = jnp.dot(hidden, down_full, preferred_element_type=jnp.float32).astype(jnp.bfloat16)
    result = result.reshape(experts, capacity, model_width)
    placed_rows, result = lax.optimization_barrier((placed_rows, result))
    returned = exchange(result)

    placed_rows = placed_rows.reshape(tiled.shape).transpose(0, 2, 1, 3).reshape(-1, model_width)
    gate_count = gate_rows.shape[0]
    placed_gate_up = placed_rows[:gate_count].reshape(w_gate_up.shape)
    placed_down = placed_rows[gate_count:].reshape(w_down.shape)

    gates = gate_probs / jnp.sum(gate_probs, axis=1, keepdims=True)
    part = jnp.sum(jnp.where(hits, gates.T[None, :, :], 0.0), axis=1).T
    rounded = lax.reduce_precision(part, exponent_bits=8, mantissa_bits=7)
    part_hi = rounded.astype(jnp.bfloat16)
    part_lo = (part - rounded).astype(jnp.bfloat16)
    both = jnp.dot(
        jnp.concatenate([part_hi, part_lo], axis=0),
        returned.reshape(slots, model_width),
        preferred_element_type=jnp.float32,
    )
    mixed_rows = both[:tok_dev] + both[tok_dev:]
    return (mixed_rows.astype(jnp.bfloat16), placed_gate_up, placed_down)


def solution(mesh):
    in_specs = (
        P(("dp", "expert"), None),
        P(("dp", "expert"), None),
        P(("dp", "expert"), None),
        P(),
        P("expert", None, "dp", None),
        P("expert", "dp", None),
    )
    out_specs = (P(("dp", "expert"), None), P("expert", None, "dp", None), P("expert", "dp", None))
    return jax.shard_map(
        per_device, mesh=mesh, in_specs=in_specs, out_specs=out_specs, check_vma=False
    )
```

```python
import jax
import jax.numpy as jnp
from jax import lax
from jax.sharding import PartitionSpec as P


def per_device(tokens, expert_ids, gate_probs, placement, w_gate_up, w_down):
    tok_dev = tokens.shape[0]
    model_width = tokens.shape[1]
    top_count = expert_ids.shape[1]
    experts = placement.shape[0]
    capacity = min(tok_dev, 3 * tok_dev * top_count // (2 * experts))
    slots = experts * capacity
    numbers = jnp.arange(experts, dtype=jnp.int32)

    owner = (placement[None, None, :] == expert_ids[:, :, None]).astype(jnp.int32)
    old_ids = jnp.sum(owner * numbers[None, None, :], axis=2)
    choice = (old_ids[:, :, None] == numbers[None, None, :]).astype(jnp.float32)
    token_hot = jnp.sum(choice, axis=1)
    earlier = (
        jnp.arange(tok_dev, dtype=jnp.int32)[None, :] < jnp.arange(tok_dev, dtype=jnp.int32)[:, None]
    ).astype(jnp.float32)
    before = jnp.dot(earlier, token_hot, preferred_element_type=jnp.float32)
    slot_of = jnp.sum(before[:, None, :] * choice, axis=2).astype(jnp.int32)
    flat_index = old_ids * capacity + slot_of
    slot_numbers = jnp.arange(slots, dtype=jnp.int32)
    hits = flat_index.T[None, :, :] == slot_numbers[:, None, None]
    pick = jnp.any(hits, axis=1).astype(jnp.bfloat16)

    def exchange(block):
        return lax.all_to_all(block, "expert", split_axis=0, concat_axis=0, tiled=True)

    gate_rows = w_gate_up.reshape(-1, model_width)
    down_rows = w_down.reshape(-1, model_width)
    shard = jnp.concatenate([gate_rows, down_rows], axis=0)
    sub, lane = 8, 128

    def tile_view(rows):
        view = rows.reshape(rows.shape[0] // sub, sub, model_width // lane, lane).transpose(0, 2, 1, 3)
        return view.reshape(experts, -1, sub, lane)

    gate_tiles = tile_view(gate_rows)
    spread = exchange(jnp.concatenate([gate_tiles, tile_view(down_rows)], axis=1))

    ring = lax.psum(1, "dp")
    parts = [shard] + [
        lax.ppermute(shard, "dp", [(j, (j + shift) % ring) for j in range(ring)])
        for shift in range(1, ring)
    ]
    local_count = w_down.shape[1]
    hidden_count = local_count * ring
    gate_up_full = jnp.concatenate(
        [part[:local_count] for part in parts] + [part[local_count:2 * local_count] for part in parts],
        axis=0,
    )
    down_full = jnp.concatenate([part[2 * local_count:] for part in parts], axis=0)

    buffer = jnp.dot(pick, tokens, preferred_element_type=jnp.float32).astype(jnp.bfloat16)
    buffer = buffer.reshape(experts, capacity, model_width)
    spread, buffer = lax.optimization_barrier((spread, buffer))
    received = exchange(buffer)

    inverse = jnp.sum(jnp.where(placement[:, None] == numbers[None, :], numbers[:, None], 0), axis=0)
    reordered = jnp.take(spread, inverse, axis=0, mode="clip")
    received, reordered = lax.optimization_barrier((received, reordered))
    placed_rows = exchange(reordered)

    row_block = received.reshape(-1, model_width)
    projected = lax.dot_general(
        row_block, gate_up_full, (((1,), (1,)), ((), ())), preferred_element_type=jnp.float32
    )
    gate_part = projected[:, :hidden_count]
    up_part = projected[:, hidden_count:]
    hidden = (jax.nn.silu(gate_part) * up_part).astype(jnp.bfloat16)
    result = jnp.dot(hidden, down_full, preferred_element_type=jnp.float32).astype(jnp.bfloat16)
    result = result.reshape(experts, capacity, model_width)
    placed_rows, result = lax.optimization_barrier((placed_rows, result))
    returned = exchange(result)

    def untile(pieces, rows):
        view = pieces.reshape(rows.shape[0] // sub, model_width // lane, sub, lane)
        return view.transpose(0, 2, 1, 3).reshape(rows.shape)

    gate_pieces = gate_tiles.shape[1]
    placed_gate_up = untile(placed_rows[:, :gate_pieces], gate_rows).reshape(w_gate_up.shape)
    placed_down = untile(placed_rows[:, gate_pieces:], down_rows).reshape(w_down.shape)

    gates = gate_probs / jnp.sum(gate_probs, axis=1, keepdims=True)
    part = jnp.sum(jnp.where(hits, gates.T[None, :, :], 0.0), axis=1).T
    rounded = lax.reduce_precision(part, exponent_bits=8, mantissa_bits=7)
    part_hi = rounded.astype(jnp.bfloat16)
    part_lo = (part - rounded).astype(jnp.bfloat16)
    both = jnp.dot(
        jnp.concatenate([part_hi, part_lo], axis=0),
        returned.reshape(slots, model_width),
        preferred_element_type=jnp.float32,
    )
    mixed_rows = both[:tok_dev] + both[tok_dev:]
    return (mixed_rows.astype(jnp.bfloat16), placed_gate_up, placed_down)


def solution(mesh):
    in_specs = (
        P(("dp", "expert"), None),
        P(("dp", "expert"), None),
        P(("dp", "expert"), None),
        P(),
        P("expert", None, "dp", None),
        P("expert", "dp", None),
    )
    out_specs = (P(("dp", "expert"), None), P("expert", None, "dp", None), P("expert", "dp", None))
    return jax.shard_map(
        per_device, mesh=mesh, in_specs=in_specs, out_specs=out_specs, check_vma=False
    )
```
